128 devices in a mesh: dp: 16 (over y, z), sub: 8 (over x, core).
Axes of the slice: x: 4, y: 4, z: 4, core: 2. Of those that a mesh axis runs over, the one named last changes fastest.
Arguments:
- attn_heads: bfloat16 [8192, 2048], P(('dp', 'sub')), may hold values from -6 to 6
- residual: bfloat16 [8192, 2048], P(('dp', 'sub')), may hold values from -6 to 6
- out_weight: bfloat16 [2048, 2048], replicated, may hold values from -0.125 to 0.125
- norm_gain: float32 [2048], replicated, may hold values from 0.1 to 1.9
- router_weight: bfloat16 [2048, 32], replicated, may hold values from -13.258252 to 13.258252
- expert_ids: int32 [8192, 8], P(('dp', 'sub')), may hold values from 0 to 31, as said below
- holders: int32 [32, 4], replicated, may hold values from 0 to 127, as said below
- slot_gate_up: bfloat16 [128, 2048, 2048], P(('dp', 'sub')), may hold values from -0.13258252 to 0.13258252, as said below
- slot_down: bfloat16 [128, 1024, 2048], P(('dp', 'sub')), may hold values from -1.5 to 1.5, as said below
- next_gain: float32 [2048], replicated, may hold values from 0.1 to 1.9
Outputs:
- new_stream: float32 [8192, 2048], P(('dp', 'sub'))
- next_normed: float32 [8192, 2048], P(('dp', 'sub'))
The draws below stay inside these ranges and needn't reach their ends.
Inputs may be any that keep to these rules, and one draw needn't show every extreme that they name: `expert_ids`: each row names 8 distinct experts. Among the rows of one device (aligned blocks of 64 rows) no expert is named more than 32 times, and one expert, drawn from the seed, is named exactly 32 times in every such block. Every device index appears exactly once in the table: each expert has 4 holders. `slot_gate_up`: devices that hold the same expert hold equal values. `slot_down`: devices that hold the same expert hold equal values.
All inputs are finite; a program needn't handle non-finite values.
Results may differ from the reference program's by a relative error of at most 0.009.
Values may be sent and summed in bfloat16 or wider, within the bound.
No kernel may reach another device: no remote copies, remote signals or barrier semaphores. Data moves between devices by JAX's collectives and lax.ppermute only.
A program may use at most 128 MiB of HBM per device.

```python
import jax
import jax.numpy as jnp
from jax import lax

D = 2048
FF = 1024
EXPERTS = 32
TOP = 8
TOK_DEV = 64
TOKENS = 8192
REPL = 4
CAP = 32


def holder_order(key):
    return jax.random.permutation(jax.random.fold_in(key, 11), EXPERTS * REPL).astype(jnp.int32)


def slot_owners(key):
    inverse = jnp.argsort(holder_order(key)).astype(jnp.int32)
    return inverse // REPL


def draw_holders(key, part):
    return holder_order(key).reshape(EXPERTS, REPL)


def draw_slot_gate_up(key, part):
    owners = slot_owners(key)
    base_key = jax.random.fold_in(key, 12)

    def single(owner):
        values = jax.random.normal(jax.random.fold_in(base_key, owner), (D, 2 * FF), jnp.float32)
        return jnp.clip(values, -6.0, 6.0) * D ** (-0.5)
    return jax.vmap(single)(owners).astype(jnp.bfloat16)


def draw_slot_down(key, part):
    owners = slot_owners(key)
    base_key = jax.random.fold_in(key, 13)

    def single(owner):
        values = jax.random.normal(jax.random.fold_in(base_key, owner), (FF, D), jnp.float32)
        return jnp.clip(values, -6.0, 6.0) * 8.0 * FF ** (-0.5)
    return jax.vmap(single)(owners).astype(jnp.bfloat16)


def draw_router_weight(key, part):
    values = jnp.clip(jax.random.normal(key, (D, EXPERTS), jnp.float32), -6.0, 6.0) * 0.45 * D ** (-0.5)
    return values.astype(jnp.bfloat16)


def draw_expert_ids(key, part):
    hot_key = jax.random.fold_in(key, 21)
    hottest = jax.random.randint(hot_key, (), 0, EXPERTS).astype(jnp.int32)
    experts_all = jnp.arange(EXPERTS, dtype=jnp.int32)
    remain = TOK_DEV * TOP - CAP

    def one_block(index):
        block_key = jax.random.fold_in(jax.random.fold_in(key, 22), index)
        shares = jax.random.randint(jax.random.fold_in(block_key, 1), (EXPERTS,), 2, 5)
        shares = jnp.where(experts_all == hottest, 0, shares)
        counts = remain * shares // jnp.sum(shares)
        left = remain - jnp.sum(counts)
        order = jax.random.permutation(jax.random.fold_in(block_key, 2), EXPERTS).astype(jnp.int32)
        position = jnp.argsort(order).astype(jnp.int32)
        hot_position = jnp.sum(jnp.where(experts_all == hottest, position, 0))
        position = position - (position > hot_position).astype(jnp.int32)
        position = jnp.where(experts_all == hottest, EXPERTS, position)
        counts = counts + (position < left).astype(jnp.int32)
        counts = jnp.where(experts_all == hottest, CAP, counts)
        bounds = jnp.cumsum(counts)
        spots = jnp.arange(TOK_DEV * TOP, dtype=jnp.int32)
        listed = jnp.sum((spots[:, None] >= bounds[None, :]).astype(jnp.int32), 1)
        table = listed.reshape(TOP, TOK_DEV).T
        shuffle = jax.random.permutation(jax.random.fold_in(block_key, 3), TOK_DEV)
        return table[shuffle]
    blocks = jax.vmap(one_block)(jnp.arange(TOKENS // TOK_DEV, dtype=jnp.int32))
    return blocks.reshape(TOKENS, TOP).astype(jnp.int32)


def block_scale(rng, shape, split, low, largest):
    level = 1.0
    for axis_at, parts in split:
        steps = jax.random.uniform(jax.random.fold_in(jax.random.fold_in(rng, 6), axis_at), (parts,), jnp.float32, low / len(split), largest / len(split))
        level = level * jnp.repeat(jnp.exp(steps), shape[axis_at] // parts).reshape((-1,) + (1,) * (len(shape) - 1 - axis_at))
    return level


def bell_draw(own_key, dims, spread, most, cuts=(), held_as=jnp.bfloat16):
    array = spread * jax.random.normal(own_key, dims, jnp.float32)
    if cuts:
        array = array * block_scale(own_key, dims, cuts, -0.22, 0.18)
    return jnp.clip(array, -most, most).astype(held_as)


def setup_inputs(seed: int = 0) -> dict:
    key_list = jax.random.split(jax.random.key(seed), 11)
    attn_heads = bell_draw(key_list[0], (TOKENS, D), 1.0, 6.0, ((0, 128),))
    residual = bell_draw(key_list[1], (TOKENS, D), 1.0, 6.0, ((0, 128),))
    out_weight = bell_draw(key_list[2], (D, D), D ** -0.5, 0.125)
    norm_gain = jnp.clip(1.0 + 0.18 * jax.random.normal(key_list[3], (D,), jnp.float32), 0.1, 1.9)
    router_weight = draw_router_weight(jax.random.fold_in(key_list[10], 71), 0)
    expert_ids = draw_expert_ids(jax.random.fold_in(key_list[10], 71), 0)
    holders = draw_holders(jax.random.fold_in(key_list[10], 71), 0)
    slot_gate_up = draw_slot_gate_up(jax.random.fold_in(key_list[10], 71), 0)
    slot_down = draw_slot_down(jax.random.fold_in(key_list[10], 71), 0)
    next_gain = jnp.clip(1.0 + 0.18 * jax.random.normal(key_list[9], (D,), jnp.float32), 0.1, 1.9)
    return dict(attn_heads=attn_heads, residual=residual, out_weight=out_weight, norm_gain=norm_gain, router_weight=router_weight, expert_ids=expert_ids, holders=holders, slot_gate_up=slot_gate_up, slot_down=slot_down, next_gain=next_gain)


def rms_factor(widened):
    return lax.rsqrt(lax.optimization_barrier(jnp.mean(widened * widened, -1, keepdims=True)) + 1e-05)

def reference(attn_heads, residual, out_weight, norm_gain, router_weight, expert_ids, holders, slot_gate_up, slot_down, next_gain):
    projected = jnp.dot(attn_heads, out_weight, preferred_element_type=jnp.float32)
    stream = residual.astype(jnp.float32) + projected
    normed = (stream * rms_factor(stream) * norm_gain).astype(jnp.bfloat16)
    logits = jnp.dot(normed, router_weight, preferred_element_type=jnp.float32)
    weights_all = jax.nn.softmax(logits, axis=-1)
    picked = jnp.take_along_axis(weights_all, expert_ids, axis=1)
    pair_count = TOKENS * TOP
    block_rows = 512
    flat_ids = expert_ids.reshape(-1).astype(jnp.int32)
    ordering = jnp.argsort(flat_ids, stable=True).astype(jnp.int32)
    sorted_rows = normed[ordering // TOP]
    sorted_rows = jnp.concatenate([sorted_rows, jnp.zeros((block_rows, D), jnp.bfloat16)], axis=0)
    counts = lax.optimization_barrier(jnp.sum((flat_ids[:, None] == jnp.arange(EXPERTS, dtype=jnp.int32)[None, :]).astype(jnp.int32), 0)).astype(jnp.int32)
    offsets = (jnp.cumsum(counts) - counts).astype(jnp.int32)
    buffer = jnp.zeros((pair_count + block_rows, D), jnp.bfloat16)

    def per_expert(expert, buffer):
        holder = holders[expert, 0].astype(jnp.int32)
        gate_up = lax.dynamic_index_in_dim(slot_gate_up, holder, 0, keepdims=False)
        down_proj = lax.dynamic_index_in_dim(slot_down, holder, 0, keepdims=False)
        start = offsets[expert]
        count = counts[expert]
        blocks = ((count + block_rows - 1) // block_rows).astype(jnp.int32)

        def per_block(index, buffer):
            first = (start + index * block_rows).astype(jnp.int32)
            inputs = lax.dynamic_slice_in_dim(sorted_rows, first, block_rows, 0)
            both_rows = jnp.dot(inputs, gate_up, preferred_element_type=jnp.float32)
            hidden = (jax.nn.silu(both_rows[:, :FF]) * both_rows[:, FF:]).astype(jnp.bfloat16)
            answer = jnp.dot(hidden, down_proj, preferred_element_type=jnp.float32).astype(jnp.bfloat16)
            keep = jnp.arange(block_rows, dtype=jnp.int32) + index * block_rows < count
            current = lax.dynamic_slice_in_dim(buffer, first, block_rows, 0)
            return lax.dynamic_update_slice_in_dim(buffer, jnp.where(keep[:, None], answer, current), first, 0)
        return lax.fori_loop(jnp.int32(0), blocks, per_block, buffer)
    buffer = lax.fori_loop(0, EXPERTS, per_expert, buffer)
    answers = jnp.zeros((pair_count, D), jnp.bfloat16).at[ordering].set(buffer[:pair_count])
    answers = answers.reshape(TOKENS, TOP, D)
    expert_sum = jnp.zeros((TOKENS, D), jnp.float32)
    for choice_index in range(TOP):
        expert_sum = expert_sum + picked[:, choice_index, None] * answers[:, choice_index, :].astype(jnp.float32)
    new_stream = stream + expert_sum
    next_normed = new_stream * rms_factor(new_stream) * next_gain
    return (new_stream, next_normed)
```

```python
import jax
import jax.numpy as jnp
from jax import lax
from jax.sharding import PartitionSpec as P


def rms_factor(widened):
    return lax.rsqrt(jnp.mean(widened * widened, -1, keepdims=True) + 1e-05)


def body(
    attn_heads,
    residual,
    out_weight,
    norm_gain,
    router_weight,
    expert_ids,
    holders,
    slot_gate_up,
    slot_down,
    next_gain,
):
    tok_count, top_count = expert_ids.shape
    expert_count, copy_count = holders.shape
    model_width = attn_heads.shape[1]
    hidden_width = slot_down.shape[1]
    device_count = lax.axis_size("dp") * lax.axis_size("sub")
    capacity = 2 * tok_count * top_count // expert_count
    per_slot = capacity // copy_count
    slot_count = device_count * per_slot
    projected = jnp.dot(attn_heads, out_weight, preferred_element_type=jnp.float32)
    stream = residual.astype(jnp.float32) + projected
    normed = (stream * rms_factor(stream) * norm_gain).astype(jnp.bfloat16)
    logits = jnp.dot(normed, router_weight, preferred_element_type=jnp.float32)
    weights_all = jax.nn.softmax(logits, axis=-1)
    chosen = expert_ids[:, :, None] == jnp.arange(expert_count, dtype=jnp.int32)[None, None, :]
    picked = jnp.sum(jnp.where(chosen, weights_all[:, None, :], 0.0), -1)
    flat_chosen = chosen.reshape(tok_count * top_count, expert_count).astype(jnp.int32)
    before = jnp.cumsum(flat_chosen, 0) - flat_chosen
    order_rank = jnp.sum(before * flat_chosen, -1)
    copy_index = order_rank % copy_count
    slot_place = order_rank // copy_count
    table_index = expert_ids.reshape(-1) * copy_count + copy_index
    table_range = jnp.arange(expert_count * copy_count, dtype=jnp.int32)
    slot_index = jnp.sum(
        jnp.where(table_index[:, None] == table_range[None, :], holders.reshape(-1)[None, :], 0), -1
    )
    target = slot_index * per_slot + slot_place
    hits = target[None, :] == jnp.arange(slot_count, dtype=jnp.int32)[:, None]
    hits = hits.reshape(slot_count, tok_count, top_count)
    send_map = jnp.any(hits, -1).astype(jnp.bfloat16)
    outgoing = jnp.dot(send_map, normed, preferred_element_type=jnp.float32).astype(jnp.bfloat16)
    outgoing = outgoing.reshape(device_count, per_slot, model_width)
    gate_up = slot_gate_up[0]
    down_proj = slot_down[0]
    packet = lax.all_to_all(outgoing, ("dp", "sub"), split_axis=0, concat_axis=0, tiled=True)
    flat_rows = packet.reshape(-1, model_width)
    both_rows = jnp.dot(flat_rows, gate_up, preferred_element_type=jnp.float32)
    hidden = (jax.nn.silu(both_rows[:, :hidden_width]) * both_rows[:, hidden_width:]).astype(
        jnp.bfloat16
    )
    answer = jnp.dot(hidden, down_proj, preferred_element_type=jnp.float32).astype(jnp.bfloat16)
    returned = lax.all_to_all(
        answer.reshape(packet.shape), ("dp", "sub"), split_axis=0, concat_axis=0, tiled=True
    )
    returned = returned.reshape(slot_count, model_width)
    mix = jnp.sum(jnp.where(hits, picked[None, :, :], 0.0), -1).T
    mix_high = lax.reduce_precision(mix, exponent_bits=8, mantissa_bits=7)
    mix_low = mix - mix_high
    mix_both = jnp.concatenate([mix_high, mix_low], 0).astype(jnp.bfloat16)
    summed = jnp.dot(mix_both, returned, preferred_element_type=jnp.float32)
    expert_sum = summed[:tok_count] + summed[tok_count:]
    new_stream = stream + expert_sum
    next_normed = new_stream * rms_factor(new_stream) * next_gain
    return (new_stream, next_normed)


def solution(mesh):
    in_specs = (
        P(("dp", "sub"), None),
        P(("dp", "sub"), None),
        P(),
        P(),
        P(),
        P(("dp", "sub"), None),
        P(),
        P(("dp", "sub"), None, None),
        P(("dp", "sub"), None, None),
        P(),
    )
    out_specs = (P(("dp", "sub"), None), P(("dp", "sub"), None))
    return jax.shard_map(body, mesh=mesh, in_specs=in_specs, out_specs=out_specs, check_vma=False)
```

```python
import jax
import jax.numpy as jnp
from jax import lax
from jax.sharding import PartitionSpec as P


def rms_factor(widened):
    return lax.rsqrt(jnp.mean(widened * widened, -1, keepdims=True) + 1e-05)


def body(
    attn_heads,
    residual,
    out_weight,
    norm_gain,
    router_weight,
    expert_ids,
    holders,
    slot_gate_up,
    slot_down,
    next_gain,
):
    tok_count, top_count = expert_ids.shape
    expert_count, copy_count = holders.shape
    model_width = attn_heads.shape[1]
    hidden_width = slot_down.shape[1]
    device_count = lax.axis_size("dp") * lax.axis_size("sub")
    capacity = 2 * tok_count * top_count // expert_count
    per_slot = capacity // copy_count
    slot_count = device_count * per_slot
    projected = jnp.dot(attn_heads, out_weight, preferred_element_type=jnp.float32)
    stream = residual.astype(jnp.float32) + projected
    normed = (stream * rms_factor(stream) * norm_gain).astype(jnp.bfloat16)
    logits = jnp.dot(normed, router_weight, preferred_element_type=jnp.float32)
    weights_all = jax.nn.softmax(logits, axis=-1)
    chosen = expert_ids[:, :, None] == jnp.arange(expert_count, dtype=jnp.int32)[None, None, :]
    picked = jnp.sum(jnp.where(chosen, weights_all[:, None, :], 0.0), -1)
    pair_count = tok_count * top_count
    flat_chosen = chosen.reshape(pair_count, expert_count)
    pair_range = jnp.arange(pair_count, dtype=jnp.int32)
    earlier = (pair_range[None, :] < pair_range[:, None]).astype(jnp.bfloat16)
    before = jnp.dot(earlier, flat_chosen.astype(jnp.bfloat16), preferred_element_type=jnp.float32)
    order_rank = jnp.sum(jnp.where(flat_chosen, before, 0.0), -1).astype(jnp.int32)
    copy_index = order_rank % copy_count
    slot_place = order_rank // copy_count
    table_index = expert_ids.reshape(-1) * copy_count + copy_index
    table_range = jnp.arange(expert_count * copy_count, dtype=jnp.int32)
    slot_index = jnp.sum(
        jnp.where(table_index[:, None] == table_range[None, :], holders.reshape(-1)[None, :], 0), -1
    )
    target = slot_index * per_slot + slot_place
    hits = target[None, :] == jnp.arange(slot_count, dtype=jnp.int32)[:, None]
    hits = hits.reshape(slot_count, tok_count, top_count)
    send_map = jnp.any(hits, -1).astype(jnp.bfloat16)
    outgoing = jnp.dot(send_map, normed, preferred_element_type=jnp.float32).astype(jnp.bfloat16)
    outgoing = outgoing.reshape(device_count, per_slot, model_width)
    gate_up = slot_gate_up[0]
    down_proj = slot_down[0]
    packet = lax.all_to_all(outgoing, ("dp", "sub"), split_axis=0, concat_axis=0, tiled=True)
    flat_rows = packet.reshape(-1, model_width)
    both_rows = jnp.dot(flat_rows, gate_up, preferred_element_type=jnp.float32)
    hidden = (jax.nn.silu(both_rows[:, :hidden_width]) * both_rows[:, hidden_width:]).astype(
        jnp.bfloat16
    )
    answer = jnp.dot(hidden, down_proj, preferred_element_type=jnp.float32).astype(jnp.bfloat16)
    returned = lax.all_to_all(
        answer.reshape(packet.shape), ("dp", "sub"), split_axis=0, concat_axis=0, tiled=True
    )
    returned = returned.reshape(slot_count, model_width)
    mix = jnp.sum(jnp.where(hits, picked[None, :, :], 0.0), -1).T
    mix_high = lax.reduce_precision(mix, exponent_bits=8, mantissa_bits=7)
    mix_low = mix - mix_high
    mix_both = jnp.concatenate([mix_high, mix_low], 0).astype(jnp.bfloat16)
    summed = jnp.dot(mix_both, returned, preferred_element_type=jnp.float32)
    expert_sum = summed[:tok_count] + summed[tok_count:]
    new_stream = stream + expert_sum
    next_normed = new_stream * rms_factor(new_stream) * next_gain
    return (new_stream, next_normed)


def solution(mesh):
    in_specs = (
        P(("dp", "sub"), None),
        P(("dp", "sub"), None),
        P(),
        P(),
        P(),
        P(("dp", "sub"), None),
        P(),
        P(("dp", "sub"), None, None),
        P(("dp", "sub"), None, None),
        P(),
    )
    out_specs = (P(("dp", "sub"), None), P(("dp", "sub"), None))
    return jax.shard_map(body, mesh=mesh, in_specs=in_specs, out_specs=out_specs, check_vma=False)
```

```python
import functools

import jax
import jax.numpy as jnp
from jax import lax
from jax.experimental import pallas as pl
from jax.experimental.pallas import tpu as pltpu
from jax.sharding import PartitionSpec as P


def rms_factor(widened):
    return lax.rsqrt(jnp.mean(widened * widened, -1, keepdims=True) + 1e-05)


def project_kernel(block, attn_ref, resid_ref, weight_ref, gain_ref, stream_ref, normed_ref, held):
    step = pl.program_id(0)
    part = jnp.dot(attn_ref[...], weight_ref[...], preferred_element_type=jnp.float32)
    part = resid_ref[...].astype(jnp.float32) + part
    stream_ref[...] = part
    held[:, pl.ds(pl.multiple_of(step * block, block), block)] = part

    @pl.when(step == pl.num_programs(0) - 1)
    def _():
        whole = held[...]
        factor = lax.rsqrt(jnp.mean(whole * whole, -1, keepdims=True) + 1e-05)
        normed_ref[...] = (whole * factor * gain_ref[...]).astype(normed_ref.dtype)


def project(attn_heads, residual, out_weight, norm_gain):
    rows, width = attn_heads.shape
    block = 512
    return pl.pallas_call(
        functools.partial(project_kernel, block),
        grid=(width // block,),
        in_specs=[
            pl.BlockSpec((rows, width), lambda j: (0, 0)),
            pl.BlockSpec((rows, block), lambda j: (0, j)),
            pl.BlockSpec((width, block), lambda j: (0, j)),
            pl.BlockSpec((1, width), lambda j: (0, 0)),
        ],
        out_specs=[
            pl.BlockSpec((rows, block), lambda j: (0, j)),
            pl.BlockSpec((rows, width), lambda j: (0, 0)),
        ],
        out_shape=[
            jax.ShapeDtypeStruct((rows, width), jnp.float32),
            jax.ShapeDtypeStruct((rows, width), jnp.bfloat16),
        ],
        scratch_shapes=[pltpu.VMEM((rows, width), jnp.float32)],
        compiler_params=pltpu.CompilerParams(dimension_semantics=("arbitrary",)),
        cost_estimate=pl.CostEstimate(
            flops=2 * rows * width * width,
            transcendentals=rows,
            bytes_accessed=2 * width * width + 2 * 2 * rows * width + 6 * rows * width,
        ),
    )(attn_heads, residual, out_weight, norm_gain.reshape(1, width))


def body(
    attn_heads,
    residual,
    out_weight,
    norm_gain,
    router_weight,
    expert_ids,
    holders,
    slot_gate_up,
    slot_down,
    next_gain,
):
    tok_count, top_count = expert_ids.shape
    expert_count, copy_count = holders.shape
    model_width = attn_heads.shape[1]
    hidden_width = slot_down.shape[1]
    device_count = lax.axis_size("dp") * lax.axis_size("sub")
    capacity = 2 * tok_count * top_count // expert_count
    per_slot = capacity // copy_count
    slot_count = device_count * per_slot
    stream, normed = project(attn_heads, residual, out_weight, norm_gain)
    logits = jnp.dot(normed, router_weight, preferred_element_type=jnp.float32)
    weights_all = jax.nn.softmax(logits, axis=-1)
    chosen = expert_ids[:, :, None] == jnp.arange(expert_count, dtype=jnp.int32)[None, None, :]
    picked = jnp.sum(jnp.where(chosen, weights_all[:, None, :], 0.0), -1)
    pair_count = tok_count * top_count
    flat_chosen = chosen.reshape(pair_count, expert_count)
    pair_range = jnp.arange(pair_count, dtype=jnp.int32)
    earlier = (pair_range[None, :] < pair_range[:, None]).astype(jnp.bfloat16)
    before = jnp.dot(earlier, flat_chosen.astype(jnp.bfloat16), preferred_element_type=jnp.float32)
    order_rank = jnp.sum(jnp.where(flat_chosen, before, 0.0), -1).astype(jnp.int32)
    copy_index = order_rank % copy_count
    slot_place = order_rank // copy_count
    table_index = expert_ids.reshape(-1) * copy_count + copy_index
    table_range = jnp.arange(expert_count * copy_count, dtype=jnp.int32)
    slot_index = jnp.sum(
        jnp.where(table_index[:, None] == table_range[None, :], holders.reshape(-1)[None, :], 0), -1
    )
    target = slot_index * per_slot + slot_place
    hits = target[None, :] == jnp.arange(slot_count, dtype=jnp.int32)[:, None]
    hits = hits.reshape(slot_count, tok_count, top_count)
    send_map = jnp.any(hits, -1).astype(jnp.bfloat16)
    outgoing = jnp.dot(send_map, normed, preferred_element_type=jnp.float32).astype(jnp.bfloat16)
    outgoing = outgoing.reshape(device_count, per_slot, model_width)
    gate_up = slot_gate_up[0]
    down_proj = slot_down[0]
    packet = lax.all_to_all(outgoing, ("dp", "sub"), split_axis=0, concat_axis=0, tiled=True)
    flat_rows = packet.reshape(-1, model_width)
    both_rows = jnp.dot(flat_rows, gate_up, preferred_element_type=jnp.float32)
    hidden = (jax.nn.silu(both_rows[:, :hidden_width]) * both_rows[:, hidden_width:]).astype(
        jnp.bfloat16
    )
    answer = jnp.dot(hidden, down_proj, preferred_element_type=jnp.float32).astype(jnp.bfloat16)
    returned = lax.all_to_all(
        answer.reshape(packet.shape), ("dp", "sub"), split_axis=0, concat_axis=0, tiled=True
    )
    returned = returned.reshape(slot_count, model_width)
    mix = jnp.sum(jnp.where(hits, picked[None, :, :], 0.0), -1).T
    mix_high = lax.reduce_precision(mix, exponent_bits=8, mantissa_bits=7)
    mix_low = mix - mix_high
    mix_both = jnp.concatenate([mix_high, mix_low], 0).astype(jnp.bfloat16)
    summed = jnp.dot(mix_both, returned, preferred_element_type=jnp.float32)
    expert_sum = summed[:tok_count] + summed[tok_count:]
    new_stream = stream + expert_sum
    next_normed = new_stream * rms_factor(new_stream) * next_gain
    return (new_stream, next_normed)


def solution(mesh):
    in_specs = (
        P(("dp", "sub"), None),
        P(("dp", "sub"), None),
        P(),
        P(),
        P(),
        P(("dp", "sub"), None),
        P(),
        P(("dp", "sub"), None, None),
        P(("dp", "sub"), None, None),
        P(),
    )
    out_specs = (P(("dp", "sub"), None), P(("dp", "sub"), None))
    return jax.shard_map(body, mesh=mesh, in_specs=in_specs, out_specs=out_specs, check_vma=False)
```

```python
import jax
import jax.numpy as jnp
from jax import lax
from jax.experimental import pallas as pl
from jax.experimental.pallas import tpu as pltpu
from jax.sharding import PartitionSpec as P


def rms_factor(widened):
    return lax.rsqrt(jnp.mean(widened * widened, -1, keepdims=True) + 1e-05)


def project_kernel(attn_ref, weight_ref, resid_ref, gain_ref, stream_ref, normed_ref, total):
    step = pl.program_id(0)
    part = jnp.dot(attn_ref[...], weight_ref[...], preferred_element_type=jnp.float32)

    @pl.when(step == 0)
    def _():
        total[...] = part

    @pl.when(step > 0)
    def _():
        total[...] += part

    @pl.when(step == pl.num_programs(0) - 1)
    def _():
        whole = resid_ref[...].astype(jnp.float32) + total[...]
        stream_ref[...] = whole
        factor = lax.rsqrt(jnp.mean(whole * whole, -1, keepdims=True) + 1e-05)
        normed_ref[...] = (whole * factor * gain_ref[...]).astype(normed_ref.dtype)


def project(attn_heads, residual, out_weight, norm_gain):
    rows, width = attn_heads.shape
    block = 512
    return pl.pallas_call(
        project_kernel,
        grid=(width // block,),
        in_specs=[
            pl.BlockSpec((rows, block), lambda k: (0, k)),
            pl.BlockSpec((block, width), lambda k: (k, 0)),
            pl.BlockSpec((rows, width), lambda k: (0, 0)),
            pl.BlockSpec((1, width), lambda k: (0, 0)),
        ],
        out_specs=[
            pl.BlockSpec((rows, width), lambda k: (0, 0)),
            pl.BlockSpec((rows, width), lambda k: (0, 0)),
        ],
        out_shape=[
            jax.ShapeDtypeStruct((rows, width), jnp.float32),
            jax.ShapeDtypeStruct((rows, width), jnp.bfloat16),
        ],
        scratch_shapes=[pltpu.VMEM((rows, width), jnp.float32)],
        compiler_params=pltpu.CompilerParams(dimension_semantics=("arbitrary",)),
        cost_estimate=pl.CostEstimate(
            flops=2 * rows * width * width,
            transcendentals=rows,
            bytes_accessed=2 * width * width + 2 * 2 * rows * width + 6 * rows * width,
        ),
    )(attn_heads, out_weight, residual, norm_gain.reshape(1, width))


def body(
    attn_heads,
    residual,
    out_weight,
    norm_gain,
    router_weight,
    expert_ids,
    holders,
    slot_gate_up,
    slot_down,
    next_gain,
):
    tok_count, top_count = expert_ids.shape
    expert_count, copy_count = holders.shape
    model_width = attn_heads.shape[1]
    hidden_width = slot_down.shape[1]
    device_count = lax.axis_size("dp") * lax.axis_size("sub")
    capacity = 2 * tok_count * top_count // expert_count
    per_slot = capacity // copy_count
    slot_count = device_count * per_slot
    stream, normed = project(attn_heads, residual, out_weight, norm_gain)
    logits = jnp.dot(normed, router_weight, preferred_element_type=jnp.float32)
    weights_all = jax.nn.softmax(logits, axis=-1)
    chosen = expert_ids[:, :, None] == jnp.arange(expert_count, dtype=jnp.int32)[None, None, :]
    picked = jnp.sum(jnp.where(chosen, weights_all[:, None, :], 0.0), -1)
    pair_count = tok_count * top_count
    flat_chosen = chosen.reshape(pair_count, expert_count)
    pair_range = jnp.arange(pair_count, dtype=jnp.int32)
    earlier = (pair_range[None, :] < pair_range[:, None]).astype(jnp.bfloat16)
    before = jnp.dot(earlier, flat_chosen.astype(jnp.bfloat16), preferred_element_type=jnp.float32)
    order_rank = jnp.sum(jnp.where(flat_chosen, before, 0.0), -1).astype(jnp.int32)
    copy_index = order_rank % copy_count
    slot_place = order_rank // copy_count
    table_index = expert_ids.reshape(-1) * copy_count + copy_index
    table_range = jnp.arange(expert_count * copy_count, dtype=jnp.int32)
    slot_index = jnp.sum(
        jnp.where(table_index[:, None] == table_range[None, :], holders.reshape(-1)[None, :], 0), -1
    )
    target = slot_index * per_slot + slot_place
    hits = target[None, :] == jnp.arange(slot_count, dtype=jnp.int32)[:, None]
    hits = hits.reshape(slot_count, tok_count, top_count)
    send_map = jnp.any(hits, -1).astype(jnp.bfloat16)
    outgoing = jnp.dot(send_map, normed, preferred_element_type=jnp.float32).astype(jnp.bfloat16)
    outgoing = outgoing.reshape(device_count, per_slot, model_width)
    gate_up = slot_gate_up[0]
    down_proj = slot_down[0]
    packet = lax.all_to_all(outgoing, ("dp", "sub"), split_axis=0, concat_axis=0, tiled=True)
    flat_rows = packet.reshape(-1, model_width)
    both_rows = jnp.dot(flat_rows, gate_up, preferred_element_type=jnp.float32)
    hidden = (jax.nn.silu(both_rows[:, :hidden_width]) * both_rows[:, hidden_width:]).astype(
        jnp.bfloat16
    )
    answer = jnp.dot(hidden, down_proj, preferred_element_type=jnp.float32).astype(jnp.bfloat16)
    returned = lax.all_to_all(
        answer.reshape(packet.shape), ("dp", "sub"), split_axis=0, concat_axis=0, tiled=True
    )
    returned = returned.reshape(slot_count, model_width)
    mix = jnp.sum(jnp.where(hits, picked[None, :, :], 0.0), -1).T
    mix_high = lax.reduce_precision(mix, exponent_bits=8, mantissa_bits=7)
    mix_low = mix - mix_high
    mix_both = jnp.concatenate([mix_high, mix_low], 0).astype(jnp.bfloat16)
    summed = jnp.dot(mix_both, returned, preferred_element_type=jnp.float32)
    expert_sum = summed[:tok_count] + summed[tok_count:]
    new_stream = stream + expert_sum
    next_normed = new_stream * rms_factor(new_stream) * next_gain
    return (new_stream, next_normed)


def solution(mesh):
    in_specs = (
        P(("dp", "sub"), None),
        P(("dp", "sub"), None),
        P(),
        P(),
        P(),
        P(("dp", "sub"), None),
        P(),
        P(("dp", "sub"), None, None),
        P(("dp", "sub"), None, None),
        P(),
    )
    out_specs = (P(("dp", "sub"), None), P(("dp", "sub"), None))
    return jax.shard_map(body, mesh=mesh, in_specs=in_specs, out_specs=out_specs, check_vma=False)
```

```python
import jax
import jax.numpy as jnp
from jax import lax
from jax.sharding import PartitionSpec as P


def rms_factor(widened):
    return lax.rsqrt(jnp.mean(widened * widened, -1, keepdims=True) + 1e-05)


def body(
    attn_heads,
    residual,
    out_weight,
    norm_gain,
    router_weight,
    expert_ids,
    holders,
    slot_gate_up,
    slot_down,
    next_gain,
):
    tok_count, top_count = expert_ids.shape
    expert_count, copy_count = holders.shape
    model_width = attn_heads.shape[1]
    hidden_width = slot_down.shape[1]
    device_count = lax.axis_size("dp") * lax.axis_size("sub")
    capacity = 2 * tok_count * top_count // expert_count
    per_slot = capacity // copy_count
    slot_count = device_count * per_slot
    projected = jnp.dot(attn_heads, out_weight, preferred_element_type=jnp.float32)
    stream = residual.astype(jnp.float32) + projected
    stream = lax.optimization_barrier(stream)
    normed = (stream * rms_factor(stream) * norm_gain).astype(jnp.bfloat16)
    logits = jnp.dot(normed, router_weight, preferred_element_type=jnp.float32)
    weights_all = jax.nn.softmax(logits, axis=-1)
    chosen = expert_ids[:, :, None] == jnp.arange(expert_count, dtype=jnp.int32)[None, None, :]
    picked = jnp.sum(jnp.where(chosen, weights_all[:, None, :], 0.0), -1)
    pair_count = tok_count * top_count
    flat_chosen = chosen.reshape(pair_count, expert_count)
    pair_range = jnp.arange(pair_count, dtype=jnp.int32)
    earlier = (pair_range[None, :] < pair_range[:, None]).astype(jnp.bfloat16)
    before = jnp.dot(earlier, flat_chosen.astype(jnp.bfloat16), preferred_element_type=jnp.float32)
    order_rank = jnp.sum(jnp.where(flat_chosen, before, 0.0), -1).astype(jnp.int32)
    copy_index = order_rank % copy_count
    slot_place = order_rank // copy_count
    table_index = expert_ids.reshape(-1) * copy_count + copy_index
    table_range = jnp.arange(expert_count * copy_count, dtype=jnp.int32)
    slot_index = jnp.sum(
        jnp.where(table_index[:, None] == table_range[None, :], holders.reshape(-1)[None, :], 0), -1
    )
    target = slot_index * per_slot + slot_place
    hits = target[None, :] == jnp.arange(slot_count, dtype=jnp.int32)[:, None]
    hits = hits.reshape(slot_count, tok_count, top_count)
    send_map = jnp.any(hits, -1).astype(jnp.bfloat16)
    outgoing = jnp.dot(send_map, normed, preferred_element_type=jnp.float32).astype(jnp.bfloat16)
    outgoing = outgoing.reshape(device_count, per_slot, model_width)
    gate_up = slot_gate_up[0]
    down_proj = slot_down[0]
    packet = lax.all_to_all(outgoing, ("dp", "sub"), split_axis=0, concat_axis=0, tiled=True)
    flat_rows = packet.reshape(-1, model_width)
    both_rows = jnp.dot(flat_rows, gate_up, preferred_element_type=jnp.float32)
    hidden = (jax.nn.silu(both_rows[:, :hidden_width]) * both_rows[:, hidden_width:]).astype(
        jnp.bfloat16
    )
    answer = jnp.dot(hidden, down_proj, preferred_element_type=jnp.float32).astype(jnp.bfloat16)
    returned = lax.all_to_all(
        answer.reshape(packet.shape), ("dp", "sub"), split_axis=0, concat_axis=0, tiled=True
    )
    returned = returned.reshape(slot_count, model_width)
    mix = jnp.sum(jnp.where(hits, picked[None, :, :], 0.0), -1).T
    mix_high = lax.reduce_precision(mix, exponent_bits=8, mantissa_bits=7)
    mix_low = mix - mix_high
    mix_both = jnp.concatenate([mix_high, mix_low], 0).astype(jnp.bfloat16)
    summed = jnp.dot(mix_both, returned, preferred_element_type=jnp.float32)
    expert_sum = summed[:tok_count] + summed[tok_count:]
    new_stream = stream + expert_sum
    next_normed = new_stream * rms_factor(new_stream) * next_gain
    return (new_stream, next_normed)


def solution(mesh):
    in_specs = (
        P(("dp", "sub"), None),
        P(("dp", "sub"), None),
        P(),
        P(),
        P(),
        P(("dp", "sub"), None),
        P(),
        P(("dp", "sub"), None, None),
        P(("dp", "sub"), None, None),
        P(),
    )
    out_specs = (P(("dp", "sub"), None), P(("dp", "sub"), None))
    return jax.shard_map(body, mesh=mesh, in_specs=in_specs, out_specs=out_specs, check_vma=False)
```

```python
import jax
import jax.numpy as jnp
from jax import lax
from jax.sharding import PartitionSpec as P


def rms_factor(widened):
    return lax.rsqrt(jnp.mean(widened * widened, -1, keepdims=True) + 1e-05)


def body(
    attn_heads,
    residual,
    out_weight,
    norm_gain,
    router_weight,
    expert_ids,
    holders,
    slot_gate_up,
    slot_down,
    next_gain,
):
    tok_count, top_count = expert_ids.shape
    expert_count, copy_count = holders.shape
    model_width = attn_heads.shape[1]
    hidden_width = slot_down.shape[1]
    device_count = lax.axis_size("dp") * lax.axis_size("sub")
    capacity = 2 * tok_count * top_count // expert_count
    per_slot = capacity // copy_count
    slot_count = device_count * per_slot
    projected = jnp.dot(attn_heads, out_weight, preferred_element_type=jnp.float32)
    stream = residual.astype(jnp.float32) + projected
    stream = lax.optimization_barrier(stream)
    normed = (stream * rms_factor(stream) * norm_gain).astype(jnp.bfloat16)
    logits = jnp.dot(normed, router_weight, preferred_element_type=jnp.float32)
    weights_all = jax.nn.softmax(logits, axis=-1)
    chosen = expert_ids[:, :, None] == jnp.arange(expert_count, dtype=jnp.int32)[None, None, :]
    picked = jnp.sum(jnp.where(chosen, weights_all[:, None, :], 0.0), -1)
    pair_count = tok_count * top_count
    flat_chosen = chosen.reshape(pair_count, expert_count)
    pair_range = jnp.arange(pair_count, dtype=jnp.int32)
    earlier = (pair_range[None, :] < pair_range[:, None]).astype(jnp.bfloat16)
    before = jnp.dot(earlier, flat_chosen.astype(jnp.bfloat16), preferred_element_type=jnp.float32)
    order_rank = jnp.sum(jnp.where(flat_chosen, before, 0.0), -1).astype(jnp.int32)
    copy_index = order_rank % copy_count
    slot_place = order_rank // copy_count
    table_index = expert_ids.reshape(-1) * copy_count + copy_index
    table_range = jnp.arange(expert_count * copy_count, dtype=jnp.int32)
    slot_index = jnp.sum(
        jnp.where(table_index[:, None] == table_range[None, :], holders.reshape(-1)[None, :], 0), -1
    )
    target = slot_index * per_slot + slot_place
    hits = target[None, :] == jnp.arange(slot_count, dtype=jnp.int32)[:, None]
    hits = hits.reshape(slot_count, tok_count, top_count)
    send_map = jnp.any(hits, -1).astype(jnp.bfloat16)
    outgoing = jnp.dot(send_map, normed, preferred_element_type=jnp.float32).astype(jnp.bfloat16)
    outgoing = outgoing.reshape(device_count, per_slot, model_width)
    gate_up = slot_gate_up[0]
    down_proj = slot_down[0]
    packet = lax.all_to_all(outgoing, ("dp", "sub"), split_axis=0, concat_axis=0, tiled=True)
    flat_rows = packet.reshape(-1, model_width)
    both_rows = jnp.dot(flat_rows, gate_up, preferred_element_type=jnp.float32)
    hidden = (jax.nn.silu(both_rows[:, :hidden_width]) * both_rows[:, hidden_width:]).astype(
        jnp.bfloat16
    )
    hidden = lax.optimization_barrier(hidden)
    answer = jnp.dot(hidden, down_proj, preferred_element_type=jnp.float32).astype(jnp.bfloat16)
    returned = lax.all_to_all(
        answer.reshape(packet.shape), ("dp", "sub"), split_axis=0, concat_axis=0, tiled=True
    )
    returned = returned.reshape(slot_count, model_width)
    mix = jnp.sum(jnp.where(hits, picked[None, :, :], 0.0), -1).T
    mix_high = lax.reduce_precision(mix, exponent_bits=8, mantissa_bits=7)
    mix_low = mix - mix_high
    mix_both = jnp.concatenate([mix_high, mix_low], 0).astype(jnp.bfloat16)
    summed = jnp.dot(mix_both, returned, preferred_element_type=jnp.float32)
    expert_sum = summed[:tok_count] + summed[tok_count:]
    new_stream = stream + expert_sum
    next_normed = new_stream * rms_factor(new_stream) * next_gain
    return (new_stream, next_normed)


def solution(mesh):
    in_specs = (
        P(("dp", "sub"), None),
        P(("dp", "sub"), None),
        P(),
        P(),
        P(),
        P(("dp", "sub"), None),
        P(),
        P(("dp", "sub"), None, None),
        P(("dp", "sub"), None, None),
        P(),
    )
    out_specs = (P(("dp", "sub"), None), P(("dp", "sub"), None))
    return jax.shard_map(body, mesh=mesh, in_specs=in_specs, out_specs=out_specs, check_vma=False)
```

```python
import jax
import jax.numpy as jnp
from jax import lax
from jax.sharding import PartitionSpec as P


def rms_factor(widened):
    return lax.rsqrt(jnp.mean(widened * widened, -1, keepdims=True) + 1e-05)


def body(
    attn_heads,
    residual,
    out_weight,
    norm_gain,
    router_weight,
    expert_ids,
    holders,
    slot_gate_up,
    slot_down,
    next_gain,
):
    tok_count, top_count = expert_ids.shape
    expert_count, copy_count = holders.shape
    model_width = attn_heads.shape[1]
    hidden_width = slot_down.shape[1]
    device_count = lax.axis_size("dp") * lax.axis_size("sub")
    capacity = 2 * tok_count * top_count // expert_count
    per_slot = capacity // copy_count
    slot_count = device_count * per_slot
    projected = jnp.dot(attn_heads, out_weight, preferred_element_type=jnp.float32)
    stream = residual.astype(jnp.float32) + projected
    stream, expert_ids, holders = lax.optimization_barrier((stream, expert_ids, holders))
    normed = (stream * rms_factor(stream) * norm_gain).astype(jnp.bfloat16)
    logits = jnp.dot(normed, router_weight, preferred_element_type=jnp.float32)
    weights_all = jax.nn.softmax(logits, axis=-1)
    chosen = expert_ids[:, :, None] == jnp.arange(expert_count, dtype=jnp.int32)[None, None, :]
    picked = jnp.sum(jnp.where(chosen, weights_all[:, None, :], 0.0), -1)
    pair_count = tok_count * top_count
    flat_chosen = chosen.reshape(pair_count, expert_count)
    pair_range = jnp.arange(pair_count, dtype=jnp.int32)
    earlier = (pair_range[None, :] < pair_range[:, None]).astype(jnp.bfloat16)
    before = jnp.dot(earlier, flat_chosen.astype(jnp.bfloat16), preferred_element_type=jnp.float32)
    order_rank = jnp.sum(jnp.where(flat_chosen, before, 0.0), -1).astype(jnp.int32)
    copy_index = order_rank % copy_count
    slot_place = order_rank // copy_count
    table_index = expert_ids.reshape(-1) * copy_count + copy_index
    table_range = jnp.arange(expert_count * copy_count, dtype=jnp.int32)
    slot_index = jnp.sum(
        jnp.where(table_index[:, None] == table_range[None, :], holders.reshape(-1)[None, :], 0), -1
    )
    target = slot_index * per_slot + slot_place
    hits = target[None, :] == jnp.arange(slot_count, dtype=jnp.int32)[:, None]
    hits = hits.reshape(slot_count, tok_count, top_count)
    send_map = jnp.any(hits, -1).astype(jnp.bfloat16)
    outgoing = jnp.dot(send_map, normed, preferred_element_type=jnp.float32).astype(jnp.bfloat16)
    outgoing = outgoing.reshape(device_count, per_slot, model_width)
    gate_up = slot_gate_up[0]
    down_proj = slot_down[0]
    packet = lax.all_to_all(outgoing, ("dp", "sub"), split_axis=0, concat_axis=0, tiled=True)
    flat_rows = packet.reshape(-1, model_width)
    both_rows = jnp.dot(flat_rows, gate_up, preferred_element_type=jnp.float32)
    hidden = (jax.nn.silu(both_rows[:, :hidden_width]) * both_rows[:, hidden_width:]).astype(
        jnp.bfloat16
    )
    answer = jnp.dot(hidden, down_proj, preferred_element_type=jnp.float32).astype(jnp.bfloat16)
    returned = lax.all_to_all(
        answer.reshape(packet.shape), ("dp", "sub"), split_axis=0, concat_axis=0, tiled=True
    )
    returned = returned.reshape(slot_count, model_width)
    mix = jnp.sum(jnp.where(hits, picked[None, :, :], 0.0), -1).T
    mix_high = lax.reduce_precision(mix, exponent_bits=8, mantissa_bits=7)
    mix_low = mix - mix_high
    mix_both = jnp.concatenate([mix_high, mix_low], 0).astype(jnp.bfloat16)
    summed = jnp.dot(mix_both, returned, preferred_element_type=jnp.float32)
    expert_sum = summed[:tok_count] + summed[tok_count:]
    new_stream = stream + expert_sum
    next_normed = new_stream * rms_factor(new_stream) * next_gain
    return (new_stream, next_normed)


def solution(mesh):
    in_specs = (
        P(("dp", "sub"), None),
        P(("dp", "sub"), None),
        P(),
        P(),
        P(),
        P(("dp", "sub"), None),
        P(),
        P(("dp", "sub"), None, None),
        P(("dp", "sub"), None, None),
        P(),
    )
    out_specs = (P(("dp", "sub"), None), P(("dp", "sub"), None))
    return jax.shard_map(body, mesh=mesh, in_specs=in_specs, out_specs=out_specs, check_vma=False)
```

```python
import jax
import jax.numpy as jnp
from jax import lax
from jax.sharding import PartitionSpec as P


def rms_factor(widened):
    return lax.rsqrt(jnp.mean(widened * widened, -1, keepdims=True) + 1e-05)


def body(
    attn_heads,
    residual,
    out_weight,
    norm_gain,
    router_weight,
    expert_ids,
    holders,
    slot_gate_up,
    slot_down,
    next_gain,
):
    tok_count, top_count = expert_ids.shape
    expert_count, copy_count = holders.shape
    model_width = attn_heads.shape[1]
    hidden_width = slot_down.shape[1]
    device_count = lax.axis_size("dp") * lax.axis_size("sub")
    capacity = 2 * tok_count * top_count // expert_count
    per_slot = capacity // copy_count
    slot_count = device_count * per_slot
    projected = jnp.dot(attn_heads, out_weight, preferred_element_type=jnp.float32)
    stream = residual.astype(jnp.float32) + projected
    stream = lax.optimization_barrier(stream)
    normed = (stream * rms_factor(stream) * norm_gain).astype(jnp.bfloat16)
    logits = jnp.dot(normed, router_weight, preferred_element_type=jnp.float32)
    weights_all = jax.nn.softmax(logits, axis=-1)
    chosen = expert_ids[:, :, None] == jnp.arange(expert_count, dtype=jnp.int32)[None, None, :]
    picked = jnp.sum(jnp.where(chosen, weights_all[:, None, :], 0.0), -1)
    pair_count = tok_count * top_count
    flat_chosen = chosen.reshape(pair_count, expert_count)
    pair_range = jnp.arange(pair_count, dtype=jnp.int32)
    earlier = (pair_range[None, :] < pair_range[:, None]).astype(jnp.bfloat16)
    before = jnp.dot(earlier, flat_chosen.astype(jnp.bfloat16), preferred_element_type=jnp.float32)
    order_rank = jnp.sum(jnp.where(flat_chosen, before, 0.0), -1).astype(jnp.int32)
    copy_index = order_rank % copy_count
    slot_place = order_rank // copy_count
    table_index = expert_ids.reshape(-1) * copy_count + copy_index
    table_range = jnp.arange(expert_count * copy_count, dtype=jnp.int32)
    slot_index = jnp.sum(
        jnp.where(table_index[:, None] == table_range[None, :], holders.reshape(-1)[None, :], 0), -1
    )
    target = slot_index * per_slot + slot_place
    hits = target[None, :] == jnp.arange(slot_count, dtype=jnp.int32)[:, None]
    hits = hits.reshape(slot_count, tok_count, top_count)
    send_map = jnp.any(hits, -1).astype(jnp.bfloat16)
    outgoing = jnp.dot(send_map, normed, preferred_element_type=jnp.float32).astype(jnp.bfloat16)
    outgoing = outgoing.reshape(device_count, per_slot, model_width)
    gate_up = slot_gate_up[0]
    down_proj = slot_down[0]
    packet = lax.all_to_all(outgoing, ("dp", "sub"), split_axis=0, concat_axis=0, tiled=True)
    flat_rows = packet.reshape(-1, model_width)
    gate_rows = jnp.dot(flat_rows, gate_up[:, :hidden_width], preferred_element_type=jnp.float32)
    up_rows = jnp.dot(flat_rows, gate_up[:, hidden_width:], preferred_element_type=jnp.float32)
    hidden = (jax.nn.silu(gate_rows) * up_rows).astype(jnp.bfloat16)
    answer = jnp.dot(hidden, down_proj, preferred_element_type=jnp.float32).astype(jnp.bfloat16)
    returned = lax.all_to_all(
        answer.reshape(packet.shape), ("dp", "sub"), split_axis=0, concat_axis=0, tiled=True
    )
    returned = returned.reshape(slot_count, model_width)
    mix = jnp.sum(jnp.where(hits, picked[None, :, :], 0.0), -1).T
    mix_high = lax.reduce_precision(mix, exponent_bits=8, mantissa_bits=7)
    mix_low = mix - mix_high
    mix_both = jnp.concatenate([mix_high, mix_low], 0).astype(jnp.bfloat16)
    summed = jnp.dot(mix_both, returned, preferred_element_type=jnp.float32)
    expert_sum = summed[:tok_count] + summed[tok_count:]
    new_stream = stream + expert_sum
    next_normed = new_stream * rms_factor(new_stream) * next_gain
    return (new_stream, next_normed)


def solution(mesh):
    in_specs = (
        P(("dp", "sub"), None),
        P(("dp", "sub"), None),
        P(),
        P(),
        P(),
        P(("dp", "sub"), None),
        P(),
        P(("dp", "sub"), None, None),
        P(("dp", "sub"), None, None),
        P(),
    )
    out_specs = (P(("dp", "sub"), None), P(("dp", "sub"), None))
    return jax.shard_map(body, mesh=mesh, in_specs=in_specs, out_specs=out_specs, check_vma=False)
```

```python
import jax
import jax.numpy as jnp
from jax import lax
from jax.sharding import PartitionSpec as P


def rms_factor(widened):
    return lax.rsqrt(jnp.mean(widened * widened, -1, keepdims=True) + 1e-05)


def body(
    attn_heads,
    residual,
    out_weight,
    norm_gain,
    router_weight,
    expert_ids,
    holders,
    slot_gate_up,
    slot_down,
    next_gain,
):
    tok_count, top_count = expert_ids.shape
    expert_count, copy_count = holders.shape
    model_width = attn_heads.shape[1]
    hidden_width = slot_down.shape[1]
    device_count = lax.axis_size("dp") * lax.axis_size("sub")
    capacity = 2 * tok_count * top_count // expert_count
    per_slot = capacity // copy_count
    slot_count = device_count * per_slot
    projected = jnp.dot(attn_heads, out_weight, preferred_element_type=jnp.float32)
    stream = residual.astype(jnp.float32) + projected
    stream = lax.optimization_barrier(stream)
    normed = (stream * rms_factor(stream) * norm_gain).astype(jnp.bfloat16)
    logits = jnp.dot(normed, router_weight, preferred_element_type=jnp.float32)
    weights_all = jax.nn.softmax(logits, axis=-1)
    chosen = expert_ids[:, :, None] == jnp.arange(expert_count, dtype=jnp.int32)[None, None, :]
    picked = jnp.sum(jnp.where(chosen, weights_all[:, None, :], 0.0), -1)
    pair_count = tok_count * top_count
    flat_chosen = chosen.reshape(pair_count, expert_count)
    pair_range = jnp.arange(pair_count, dtype=jnp.int32)
    earlier = (pair_range[None, :] < pair_range[:, None]).astype(jnp.bfloat16)
    before = jnp.dot(earlier, flat_chosen.astype(jnp.bfloat16), preferred_element_type=jnp.float32)
    order_rank = jnp.sum(jnp.where(flat_chosen, before, 0.0), -1).astype(jnp.int32)
    copy_index = order_rank % copy_count
    slot_place = order_rank // copy_count
    table_index = expert_ids.reshape(-1) * copy_count + copy_index
    table_range = jnp.arange(expert_count * copy_count, dtype=jnp.int32)
    slot_index = jnp.sum(
        jnp.where(table_index[:, None] == table_range[None, :], holders.reshape(-1)[None, :], 0), -1
    )
    target = slot_index * per_slot + slot_place
    hits = target[None, :] == jnp.arange(slot_count, dtype=jnp.int32)[:, None]
    hits = hits.reshape(slot_count, tok_count, top_count)
    send_map = jnp.any(hits, -1).astype(jnp.bfloat16)
    outgoing = jnp.dot(send_map, normed, preferred_element_type=jnp.float32).astype(jnp.bfloat16)
    outgoing = outgoing.reshape(device_count, per_slot, model_width)
    gate_up = slot_gate_up[0]
    down_proj = slot_down[0]
    packet = lax.all_to_all(outgoing, ("dp", "sub"), split_axis=0, concat_axis=0, tiled=True)
    flat_rows = packet.reshape(-1, model_width)
    both_rows = jnp.dot(flat_rows, gate_up, preferred_element_type=jnp.float32)
    hidden = (jax.nn.silu(both_rows[:, :hidden_width]) * both_rows[:, hidden_width:]).astype(
        jnp.bfloat16
    )
    answer = jnp.dot(hidden, down_proj, preferred_element_type=jnp.float32).astype(jnp.bfloat16)
    returned = lax.all_to_all(
        answer.reshape(packet.shape), ("dp", "sub"), split_axis=0, concat_axis=0, tiled=True
    )
    returned = returned.reshape(slot_count, model_width)
    mix = jnp.sum(jnp.where(hits, picked[None, :, :], 0.0), -1).T
    expert_sum = jnp.dot(mix.astype(jnp.bfloat16), returned, preferred_element_type=jnp.float32)
    new_stream = stream + expert_sum
    next_normed = new_stream * rms_factor(new_stream) * next_gain
    return (new_stream, next_normed)


def solution(mesh):
    in_specs = (
        P(("dp", "sub"), None),
        P(("dp", "sub"), None),
        P(),
        P(),
        P(),
        P(("dp", "sub"), None),
        P(),
        P(("dp", "sub"), None, None),
        P(("dp", "sub"), None, None),
        P(),
    )
    out_specs = (P(("dp", "sub"), None), P(("dp", "sub"), None))
    return jax.shard_map(body, mesh=mesh, in_specs=in_specs, out_specs=out_specs, check_vma=False)
```
